512 devices in a mesh: bl: 128 (over y, z_hi, x, core), ta: 4 (over z_lo).
Axes of the slice: x: 4, y: 8, z: 8 (z_hi: 2, z_lo: 4; z = z_hi * 4 + z_lo), core: 2. Of those that a mesh axis runs over, the one named last changes fastest.
Arguments:
- visibility: bfloat16 [2, 8, 16384, 1024], P(None, 'ta', 'bl'), may hold values from -6 to 6
- delay_kbin: int32 [1024], replicated, may hold values from 0 to 511
- block_bin: int32 [128], replicated, may hold values from 0 to 127
- bin_slot: int32 [128], replicated, may hold values from 0 to 127, each once
- pair_flags: int32 [8, 128], replicated, may hold values 0 or 1
Outputs:
- bandpower: float32 [128, 512], P('bl')
The draws below stay inside these ranges and needn't reach their ends.
Inputs may be any that keep to these rules, and one draw needn't show every extreme that they name: `bin_slot`: each row number once.
All inputs are finite; a program needn't handle non-finite values.
Results may differ from the reference program's by a relative error of at most 0.0055.
Values may be sent and summed in bfloat16 or wider, within the bound.
No kernel may reach another device: no remote copies, remote signals or barrier semaphores. Data moves between devices by JAX's collectives and lax.ppermute only.
A program may use at most 64 MiB of HBM per device.

```python
import math
import jax
import jax.numpy as jnp
from jax import lax

NCH = 1024
BL_DEV = 128
NK = 512
NBLK = 128
NBB = 128
TIMES = 8
CYCLE = 8


def place_ends(values, key, low, largest):
    shape = values.shape
    spot = [jax.random.randint(jax.random.fold_in(key, axis), (), 0, shape[axis]) for axis in range(len(shape))]
    values = values.at[tuple(spot)].set(low)
    longest = shape.index(max(shape))
    spot[longest] = (spot[longest] + 1) % shape[longest]
    return values.at[tuple(spot)].set(largest)


def block_levels(stream_key, shape, cuts, smallest, high):
    def one(dim, blocks):
        steps = jax.random.uniform(jax.random.fold_in(jax.random.fold_in(stream_key, 6), dim), (blocks,), jnp.float32, smallest / len(cuts), high / len(cuts))
        return jnp.repeat(jnp.exp(steps), shape[dim] // blocks).reshape((-1,) + (1,) * (len(shape) - dim - 1))

    gain = one(*cuts[0])
    for cut in cuts[1:]:
        gain = gain * one(*cut)
    return gain


def normal_values(rng, dims, width, most, split=(), held_as=jnp.bfloat16):
    loudness = block_levels(rng, dims, split, -0.22, 0.18) if split else 1.0
    array = jax.random.normal(rng, dims, jnp.float32) * width * loudness
    return jnp.minimum(jnp.maximum(array, -most), most).astype(held_as)


def setup_inputs(seed: int = 0) -> dict:
    keys = jax.random.split(jax.random.key(seed), 6)
    visibility = normal_values(keys[0], (2, TIMES, NBLK * BL_DEV, NCH), 1.0, 6.0, ((1, 4), (2, 128)))
    delay_kbin = place_ends(jax.random.randint(keys[1], (NCH,), 0, NK), jax.random.fold_in(keys[1], 1), 0, NK - 1).astype(jnp.int32)
    block_bin = place_ends(jax.random.randint(keys[2], (NBLK,), 0, NBB), jax.random.fold_in(keys[2], 1), 0, NBB - 1).astype(jnp.int32)
    bin_slot = jax.random.permutation(keys[3], NBB).astype(jnp.int32)
    pair_flags = place_ends((jax.random.randint(keys[4], (CYCLE, NBLK), 0, 2) < 1).astype(jnp.int32), jax.random.fold_in(keys[4], 1), 0, 1)
    return dict(visibility=visibility, delay_kbin=delay_kbin, block_bin=block_bin, bin_slot=bin_slot, pair_flags=pair_flags)


def delay_tables(num_chans):
    chan_idx = jnp.arange(num_chans, dtype=jnp.int32)
    phase_idx = chan_idx[:, None] * chan_idx[None, :] % num_chans
    step_angle = 2.0 * math.pi / num_chans
    phase_angle = step_angle * phase_idx.astype(jnp.float32)
    base_angle = step_angle * chan_idx.astype(jnp.float32)
    taper_win = 0.35875 - 0.48829 * jnp.cos(base_angle) + 0.14128 * jnp.cos(2.0 * base_angle) - 0.01168 * jnp.cos(3.0 * base_angle)
    scale_norm = 1.0 / jnp.sqrt(jnp.sum(taper_win * taper_win))
    weight_col = (taper_win * scale_norm)[:, None]
    cos_tab = (weight_col * jnp.cos(phase_angle)).astype(jnp.bfloat16)
    sin_tab = (weight_col * jnp.sin(phase_angle)).astype(jnp.bfloat16)
    return (cos_tab, sin_tab)

def delay_transform(block_data, cos_tab, sin_tab):
    num_rows = block_data.shape[1]
    flat_rows = block_data.reshape(2 * num_rows, block_data.shape[2])
    cos_part = jnp.dot(flat_rows, cos_tab, preferred_element_type=jnp.float32).reshape(2, num_rows, -1)
    sin_part = jnp.dot(flat_rows, sin_tab, preferred_element_type=jnp.float32).reshape(2, num_rows, -1)
    real_part = cos_part[0] + sin_part[1]
    imag_part = cos_part[1] - sin_part[0]
    return jnp.stack([real_part, imag_part]).astype(jnp.bfloat16)

def cross_power(own_block, other_block):
    own_f = own_block.astype(jnp.float32)
    other_f = other_block.astype(jnp.float32)
    return lax.optimization_barrier(jnp.sum(own_f[0] * other_f[0] + own_f[1] * other_f[1], axis=0))

def reference(visibility, delay_kbin, block_bin, bin_slot, pair_flags):
    cos_tab, sin_tab = delay_tables(NCH)
    blocks = visibility.reshape(2, TIMES, NBLK, BL_DEV, NCH).transpose(2, 0, 1, 3, 4).reshape(NBLK, 2, TIMES * BL_DEV, NCH)
    spectra = lax.map(lambda one_block: delay_transform(one_block, cos_tab, sin_tab), blocks)

    def block_power(block_id):
        own_block = spectra[block_id]
        power_sum = jnp.zeros((NCH,), jnp.float32)
        for offset in range(CYCLE):
            partner_idx = ((block_id - offset - 1) % NBLK).astype(jnp.int32)
            flag_value = pair_flags[offset, block_id].astype(jnp.float32)
            power_sum = power_sum + flag_value * cross_power(own_block, spectra[partner_idx])
        return power_sum
    powers = lax.map(block_power, jnp.arange(NBLK, dtype=jnp.int32))
    k_onehot = (delay_kbin[:, None] == jnp.arange(NK, dtype=jnp.int32)[None, :]).astype(jnp.float32)
    binned = jnp.dot(powers, k_onehot, precision=lax.Precision.HIGHEST) * (1.0 / math.sqrt(BL_DEV * TIMES))
    slot_onehot = (bin_slot[block_bin][None, :] == jnp.arange(NBB, dtype=jnp.int32)[:, None]).astype(jnp.float32)
    return jnp.dot(slot_onehot, binned, precision=lax.Precision.HIGHEST)
```

```python
import math

import jax
import jax.numpy as jnp
from jax import lax
from jax.sharding import PartitionSpec as P


def shifted(block, axis, distance):
    devices = range(lax.axis_size(axis))
    route = [((i - distance) % len(devices), i) for i in devices]
    return lax.ppermute(block, axis, route)


def delay_tables(num_chans):
    chan_idx = jnp.arange(num_chans, dtype=jnp.int32)
    phase_idx = chan_idx[:, None] * chan_idx[None, :] % num_chans
    step_angle = 2.0 * math.pi / num_chans
    phase_angle = step_angle * phase_idx.astype(jnp.float32)
    base_angle = step_angle * chan_idx.astype(jnp.float32)
    taper_win = (
        0.35875
        - 0.48829 * jnp.cos(base_angle)
        + 0.14128 * jnp.cos(2.0 * base_angle)
        - 0.01168 * jnp.cos(3.0 * base_angle)
    )
    scale_norm = 1.0 / jnp.sqrt(jnp.sum(taper_win * taper_win))
    weight_col = (taper_win * scale_norm)[:, None]
    cos_tab = (weight_col * jnp.cos(phase_angle)).astype(jnp.bfloat16)
    sin_tab = (weight_col * jnp.sin(phase_angle)).astype(jnp.bfloat16)
    return (cos_tab, sin_tab)


def delay_transform(block_data, cos_tab, sin_tab):
    num_rows = block_data.shape[1]
    flat_rows = block_data.reshape(2 * num_rows, block_data.shape[2])
    cos_part = jnp.dot(flat_rows, cos_tab, preferred_element_type=jnp.float32).reshape(
        2, num_rows, -1
    )
    sin_part = jnp.dot(flat_rows, sin_tab, preferred_element_type=jnp.float32).reshape(
        2, num_rows, -1
    )
    real_part = cos_part[0] + sin_part[1]
    imag_part = cos_part[1] - sin_part[0]
    return jnp.stack([real_part, imag_part]).astype(jnp.bfloat16)


def cross_power(own_block, other_block):
    own_f = own_block.astype(jnp.float32)
    other_f = other_block.astype(jnp.float32)
    return jnp.sum(own_f[0] * other_f[0] + own_f[1] * other_f[1], axis=0)


def accumulate(power_sum, flag_value, own_block, partner):
    return power_sum + flag_value.astype(jnp.float32) * cross_power(own_block, partner)


def per_device(visibility, delay_kbin, block_bin, bin_slot, pair_flags):
    num_times = visibility.shape[1]
    num_rows = visibility.shape[2]
    num_chans = visibility.shape[3]
    num_kbins = num_chans // 2
    num_bins = bin_slot.shape[0]
    cycle_len = pair_flags.shape[0]
    cos_tab, sin_tab = delay_tables(num_chans)
    spectra = delay_transform(
        visibility.reshape(2, num_times * num_rows, num_chans), cos_tab, sin_tab
    )
    my_block = lax.axis_index("bl")
    my_flags = lax.dynamic_index_in_dim(pair_flags, my_block, axis=1, keepdims=False)
    my_bin = lax.dynamic_index_in_dim(block_bin, my_block, axis=0, keepdims=False)
    power_sum = jnp.zeros((num_chans,), jnp.float32)
    moving = spectra
    for offset in range(cycle_len):
        moving = shifted(moving, "bl", 1)
        power_sum = accumulate(power_sum, my_flags[offset], spectra, moving)
    k_onehot = (delay_kbin[:, None] == jnp.arange(num_kbins, dtype=jnp.int32)[None, :]).astype(
        jnp.float32
    )
    scale_value = 1.0 / math.sqrt(num_rows * num_times * lax.axis_size("ta"))
    binned = jnp.dot(power_sum[None, :], k_onehot, precision=lax.Precision.HIGHEST)[0] * scale_value
    target_row = jnp.sum(jnp.where(jnp.arange(num_bins, dtype=jnp.int32) == my_bin, bin_slot, 0))
    slot_onehot = (jnp.arange(num_bins, dtype=jnp.int32) == target_row).astype(jnp.float32)
    partial_table = slot_onehot[:, None] * lax.psum(binned, "ta")[None, :]
    received = lax.all_to_all(partial_table, "bl", 0, 0, tiled=True)
    return jnp.sum(received, axis=0, keepdims=True)


def solution(mesh):
    placed = (P(None, "ta", "bl", None), P(), P(), P(), P())
    return jax.shard_map(
        per_device, mesh=mesh, in_specs=placed, out_specs=P("bl", None), check_vma=False
    )
```

```python
import math

import jax
import jax.numpy as jnp
from jax import lax
from jax.sharding import PartitionSpec as P


def shifted(block, axis, distance):
    devices = range(lax.axis_size(axis))
    route = [((i - distance) % len(devices), i) for i in devices]
    return lax.ppermute(block, axis, route)


def delay_tables(num_chans):
    chan_idx = jnp.arange(num_chans, dtype=jnp.int32)
    phase_idx = chan_idx[:, None] * chan_idx[None, :] % num_chans
    step_angle = 2.0 * math.pi / num_chans
    phase_angle = step_angle * phase_idx.astype(jnp.float32)
    base_angle = step_angle * chan_idx.astype(jnp.float32)
    taper_win = (
        0.35875
        - 0.48829 * jnp.cos(base_angle)
        + 0.14128 * jnp.cos(2.0 * base_angle)
        - 0.01168 * jnp.cos(3.0 * base_angle)
    )
    scale_norm = 1.0 / jnp.sqrt(jnp.sum(taper_win * taper_win))
    weight_col = (taper_win * scale_norm)[:, None]
    cos_tab = (weight_col * jnp.cos(phase_angle)).astype(jnp.bfloat16)
    sin_tab = (weight_col * jnp.sin(phase_angle)).astype(jnp.bfloat16)
    return (cos_tab, sin_tab)


def delay_transform(block_data, cos_tab, sin_tab):
    num_rows = block_data.shape[1]
    flat_rows = block_data.reshape(2 * num_rows, block_data.shape[2])
    cos_part = jnp.dot(flat_rows, cos_tab, preferred_element_type=jnp.float32).reshape(
        2, num_rows, -1
    )
    sin_part = jnp.dot(flat_rows, sin_tab, preferred_element_type=jnp.float32).reshape(
        2, num_rows, -1
    )
    real_part = cos_part[0] + sin_part[1]
    imag_part = cos_part[1] - sin_part[0]
    return jnp.stack([real_part, imag_part]).astype(jnp.bfloat16)


def cross_power(own_block, other_block):
    own_f = own_block.astype(jnp.float32)
    other_f = other_block.astype(jnp.float32)
    return jnp.sum(own_f[0] * other_f[0] + own_f[1] * other_f[1], axis=0)


def accumulate(power_sum, flag_value, own_block, partner):
    return power_sum + flag_value.astype(jnp.float32) * cross_power(own_block, partner)


def per_device(visibility, delay_kbin, block_bin, bin_slot, pair_flags):
    num_times = visibility.shape[1]
    num_rows = visibility.shape[2]
    num_chans = visibility.shape[3]
    num_kbins = num_chans // 2
    num_bins = bin_slot.shape[0]
    cycle_len = pair_flags.shape[0]
    cos_tab, sin_tab = delay_tables(num_chans)
    spectra = delay_transform(
        visibility.reshape(2, num_times * num_rows, num_chans), cos_tab, sin_tab
    )
    my_block = lax.axis_index("bl")
    num_blocks = lax.axis_size("bl")
    half = cycle_len // 2
    flags_window = lax.dynamic_slice_in_dim(
        jnp.concatenate([pair_flags, pair_flags], axis=1), my_block, half + 1, axis=1
    )
    bins_window = lax.dynamic_slice_in_dim(
        jnp.concatenate([block_bin, block_bin]), my_block, half + 1
    )
    power_rows = [jnp.zeros((num_chans,), jnp.float32) for _ in range(half + 1)]
    below = spectra
    above = spectra
    for step in range(1, half + 1):
        below = shifted(below, "bl", 1)
        previous_above = above
        above = shifted(above, "bl", -1)
        odd = 2 * step - 1
        power_rows[step - 1] = accumulate(
            power_rows[step - 1], flags_window[odd - 1, step - 1], previous_above, below
        )
        power_rows[step] = accumulate(
            power_rows[step], flags_window[odd, step], above, below
        )
    power_table = jnp.stack(power_rows)
    k_onehot = (delay_kbin[:, None] == jnp.arange(num_kbins, dtype=jnp.int32)[None, :]).astype(
        jnp.float32
    )
    scale_value = 1.0 / math.sqrt(num_rows * num_times * lax.axis_size("ta"))
    binned = jnp.dot(power_table, k_onehot, precision=lax.Precision.HIGHEST) * scale_value
    binned = lax.psum(binned, "ta")
    target_rows = bin_slot[bins_window]
    slot_onehot = (
        jnp.arange(num_bins, dtype=jnp.int32)[:, None] == target_rows[None, :]
    ).astype(jnp.float32)
    partial_table = jnp.sum(slot_onehot[:, :, None] * binned[None, :, :], axis=1)
    received = lax.all_to_all(partial_table, "bl", 0, 0, tiled=True)
    return jnp.sum(received, axis=0, keepdims=True)


def solution(mesh):
    placed = (P(None, "ta", "bl", None), P(), P(), P(), P())
    return jax.shard_map(
        per_device, mesh=mesh, in_specs=placed, out_specs=P("bl", None), check_vma=False
    )
```

```python
import math

import ml_dtypes
import numpy as np

import jax
import jax.numpy as jnp
from jax import lax
from jax.sharding import PartitionSpec as P


def shifted(block, axis, distance):
    devices = range(lax.axis_size(axis))
    route = [((i - distance) % len(devices), i) for i in devices]
    return lax.ppermute(block, axis, route)


def delay_tables(num_chans):
    chan_idx = np.arange(num_chans, dtype=np.int32)
    phase_idx = chan_idx[:, None] * chan_idx[None, :] % num_chans
    step_angle = np.float32(2.0 * math.pi / num_chans)
    phase_angle = step_angle * phase_idx.astype(np.float32)
    base_angle = step_angle * chan_idx.astype(np.float32)

    def cos32(angle):
        return np.cos(angle.astype(np.float64)).astype(np.float32)

    taper_win = (
        np.float32(0.35875)
        - np.float32(0.48829) * cos32(base_angle)
        + np.float32(0.14128) * cos32(np.float32(2.0) * base_angle)
        - np.float32(0.01168) * cos32(np.float32(3.0) * base_angle)
    )
    scale_norm = np.float32(1.0) / np.sqrt(np.sum(taper_win * taper_win, dtype=np.float32))
    weight_col = (taper_win * scale_norm)[:, None]
    cos_tab = (weight_col * cos32(phase_angle)).astype(ml_dtypes.bfloat16)
    sin_tab = (weight_col * np.sin(phase_angle.astype(np.float64)).astype(np.float32)).astype(
        ml_dtypes.bfloat16
    )
    return (jnp.asarray(cos_tab), jnp.asarray(sin_tab))


def delay_transform(block_data, cos_tab, sin_tab):
    num_rows = block_data.shape[1]
    flat_rows = block_data.reshape(2 * num_rows, block_data.shape[2])
    cos_part = jnp.dot(flat_rows, cos_tab, preferred_element_type=jnp.float32).reshape(
        2, num_rows, -1
    )
    sin_part = jnp.dot(flat_rows, sin_tab, preferred_element_type=jnp.float32).reshape(
        2, num_rows, -1
    )
    real_part = cos_part[0] + sin_part[1]
    imag_part = cos_part[1] - sin_part[0]
    return jnp.stack([real_part, imag_part]).astype(jnp.bfloat16)


def cross_power(own_block, other_block):
    own_f = own_block.astype(jnp.float32)
    other_f = other_block.astype(jnp.float32)
    return jnp.sum(own_f[0] * other_f[0] + own_f[1] * other_f[1], axis=0)


def accumulate(power_sum, flag_value, own_block, partner):
    return power_sum + flag_value.astype(jnp.float32) * cross_power(own_block, partner)


def per_device(visibility, delay_kbin, block_bin, bin_slot, pair_flags):
    num_times = visibility.shape[1]
    num_rows = visibility.shape[2]
    num_chans = visibility.shape[3]
    num_kbins = num_chans // 2
    num_bins = bin_slot.shape[0]
    cycle_len = pair_flags.shape[0]
    cos_tab, sin_tab = delay_tables(num_chans)
    spectra = delay_transform(
        visibility.reshape(2, num_times * num_rows, num_chans), cos_tab, sin_tab
    )
    my_block = lax.axis_index("bl")
    num_blocks = lax.axis_size("bl")
    half = cycle_len // 2
    flags_window = lax.dynamic_slice_in_dim(
        jnp.concatenate([pair_flags, pair_flags], axis=1), my_block, half + 1, axis=1
    )
    bins_window = lax.dynamic_slice_in_dim(
        jnp.concatenate([block_bin, block_bin]), my_block, half + 1
    )
    power_rows = [jnp.zeros((num_chans,), jnp.float32) for _ in range(half + 1)]
    below = spectra
    above = spectra
    for step in range(1, half + 1):
        below = shifted(below, "bl", 1)
        previous_above = above
        above = shifted(above, "bl", -1)
        odd = 2 * step - 1
        power_rows[step - 1] = accumulate(
            power_rows[step - 1], flags_window[odd - 1, step - 1], previous_above, below
        )
        power_rows[step] = accumulate(
            power_rows[step], flags_window[odd, step], above, below
        )
    power_table = jnp.stack(power_rows)
    k_onehot = (delay_kbin[:, None] == jnp.arange(num_kbins, dtype=jnp.int32)[None, :]).astype(
        jnp.float32
    )
    scale_value = 1.0 / math.sqrt(num_rows * num_times * lax.axis_size("ta"))
    binned = jnp.dot(power_table, k_onehot, precision=lax.Precision.HIGHEST) * scale_value
    binned = lax.psum(binned, "ta")
    target_rows = bin_slot[bins_window]
    slot_onehot = (
        jnp.arange(num_bins, dtype=jnp.int32)[:, None] == target_rows[None, :]
    ).astype(jnp.float32)
    partial_table = jnp.sum(slot_onehot[:, :, None] * binned[None, :, :], axis=1)
    received = lax.all_to_all(partial_table, "bl", 0, 0, tiled=True)
    return jnp.sum(received, axis=0, keepdims=True)


def solution(mesh):
    placed = (P(None, "ta", "bl", None), P(), P(), P(), P())
    return jax.shard_map(
        per_device, mesh=mesh, in_specs=placed, out_specs=P("bl", None), check_vma=False
    )
```

```python
import math

import ml_dtypes
import numpy as np

import jax
import jax.numpy as jnp
from jax import lax
from jax.sharding import PartitionSpec as P


def shifted(block, axis, distance):
    devices = range(lax.axis_size(axis))
    route = [((i - distance) % len(devices), i) for i in devices]
    return lax.ppermute(block, axis, route)


def delay_tables(num_chans):
    chan_idx = np.arange(num_chans, dtype=np.int32)
    phase_idx = chan_idx[:, None] * chan_idx[None, :] % num_chans
    step_angle = np.float32(2.0 * math.pi / num_chans)
    phase_angle = step_angle * phase_idx.astype(np.float32)
    base_angle = step_angle * chan_idx.astype(np.float32)

    def cos32(angle):
        return np.cos(angle.astype(np.float64)).astype(np.float32)

    taper_win = (
        np.float32(0.35875)
        - np.float32(0.48829) * cos32(base_angle)
        + np.float32(0.14128) * cos32(np.float32(2.0) * base_angle)
        - np.float32(0.01168) * cos32(np.float32(3.0) * base_angle)
    )
    scale_norm = np.float32(1.0) / np.sqrt(np.sum(taper_win * taper_win, dtype=np.float32))
    weight_col = (taper_win * scale_norm)[:, None]
    cos_tab = (weight_col * cos32(phase_angle)).astype(ml_dtypes.bfloat16)
    sin_tab = (weight_col * np.sin(phase_angle.astype(np.float64)).astype(np.float32)).astype(
        ml_dtypes.bfloat16
    )
    return (jnp.asarray(cos_tab), jnp.asarray(sin_tab))


def delay_transform(block_data, cos_tab, sin_tab):
    num_rows = block_data.shape[1]
    flat_rows = block_data.reshape(2 * num_rows, block_data.shape[2])
    cos_part = jnp.dot(flat_rows, cos_tab, preferred_element_type=jnp.float32).reshape(
        2, num_rows, -1
    )
    sin_part = jnp.dot(flat_rows, sin_tab, preferred_element_type=jnp.float32).reshape(
        2, num_rows, -1
    )
    real_part = cos_part[0] + sin_part[1]
    imag_part = cos_part[1] - sin_part[0]
    return jnp.stack([real_part, imag_part]).astype(jnp.bfloat16)


def cross_power(own_block, other_block):
    own_f = own_block.astype(jnp.float32)
    other_f = other_block.astype(jnp.float32)
    return jnp.sum(own_f[0] * other_f[0] + own_f[1] * other_f[1], axis=0)


def accumulate(power_sum, flag_value, own_block, partner):
    return power_sum + flag_value.astype(jnp.float32) * cross_power(own_block, partner)


def per_device(visibility, delay_kbin, block_bin, bin_slot, pair_flags):
    num_times = visibility.shape[1]
    num_rows = visibility.shape[2]
    num_chans = visibility.shape[3]
    num_kbins = num_chans // 2
    num_bins = bin_slot.shape[0]
    cycle_len = pair_flags.shape[0]
    cos_tab, sin_tab = delay_tables(num_chans)
    spectra = delay_transform(
        visibility.reshape(2, num_times * num_rows, num_chans), cos_tab, sin_tab
    )
    my_block = lax.axis_index("bl")
    num_blocks = lax.axis_size("bl")
    half = cycle_len // 2
    flags_window = lax.dynamic_slice_in_dim(
        jnp.concatenate([pair_flags, pair_flags], axis=1), my_block, half + 1, axis=1
    )
    bins_window = lax.dynamic_slice_in_dim(
        jnp.concatenate([block_bin, block_bin]), my_block, half + 1
    )
    power_rows = [jnp.zeros((num_chans,), jnp.float32) for _ in range(half + 1)]
    below = spectra
    above = spectra
    for step in range(1, half + 1):
        below = shifted(below, "bl", 1)
        previous_above = above
        above = shifted(above, "bl", -1)
        odd = 2 * step - 1
        power_rows[step - 1] = accumulate(
            power_rows[step - 1], flags_window[odd - 1, step - 1], previous_above, below
        )
        power_rows[step] = accumulate(
            power_rows[step], flags_window[odd, step], above, below
        )
    power_table = jnp.stack(power_rows)
    k_onehot = (delay_kbin[:, None] == jnp.arange(num_kbins, dtype=jnp.int32)[None, :]).astype(
        jnp.float32
    )
    scale_value = 1.0 / math.sqrt(num_rows * num_times * lax.axis_size("ta"))
    binned = jnp.dot(power_table, k_onehot, precision=lax.Precision.HIGHEST) * scale_value
    target_rows = bin_slot[bins_window]
    slot_onehot = (
        jnp.arange(num_bins, dtype=jnp.int32)[:, None] == target_rows[None, :]
    ).astype(jnp.float32)
    partial_table = jnp.sum(slot_onehot[:, :, None] * binned[None, :, :], axis=1)
    received = lax.all_to_all(partial_table, "bl", 0, 0, tiled=True)
    return lax.psum(jnp.sum(received, axis=0, keepdims=True), "ta")


def solution(mesh):
    placed = (P(None, "ta", "bl", None), P(), P(), P(), P())
    return jax.shard_map(
        per_device, mesh=mesh, in_specs=placed, out_specs=P("bl", None), check_vma=False
    )
```

```python
import math

import ml_dtypes
import numpy as np

import jax
import jax.numpy as jnp
from jax import lax
from jax.sharding import PartitionSpec as P


def shifted(block, axis, distance):
    devices = range(lax.axis_size(axis))
    route = [((i - distance) % len(devices), i) for i in devices]
    return lax.ppermute(block, axis, route)


def group_shifted(block, axis, group, distance):
    devices = range(lax.axis_size(axis))
    route = [(i, i - i % group + (i + distance) % group) for i in devices]
    return lax.ppermute(block, axis, route)


def delay_tables(num_chans):
    chan_idx = np.arange(num_chans, dtype=np.int32)
    phase_idx = chan_idx[:, None] * chan_idx[None, :] % num_chans
    step_angle = np.float32(2.0 * math.pi / num_chans)
    phase_angle = step_angle * phase_idx.astype(np.float32)
    base_angle = step_angle * chan_idx.astype(np.float32)

    def cos32(angle):
        return np.cos(angle.astype(np.float64)).astype(np.float32)

    taper_win = (
        np.float32(0.35875)
        - np.float32(0.48829) * cos32(base_angle)
        + np.float32(0.14128) * cos32(np.float32(2.0) * base_angle)
        - np.float32(0.01168) * cos32(np.float32(3.0) * base_angle)
    )
    scale_norm = np.float32(1.0) / np.sqrt(np.sum(taper_win * taper_win, dtype=np.float32))
    weight_col = (taper_win * scale_norm)[:, None]
    cos_tab = (weight_col * cos32(phase_angle)).astype(ml_dtypes.bfloat16)
    sin_tab = (weight_col * np.sin(phase_angle.astype(np.float64)).astype(np.float32)).astype(
        ml_dtypes.bfloat16
    )
    return (jnp.asarray(cos_tab), jnp.asarray(sin_tab))


def delay_transform(block_data, cos_tab, sin_tab):
    num_rows = block_data.shape[1]
    flat_rows = block_data.reshape(2 * num_rows, block_data.shape[2])
    cos_part = jnp.dot(flat_rows, cos_tab, preferred_element_type=jnp.float32).reshape(
        2, num_rows, -1
    )
    sin_part = jnp.dot(flat_rows, sin_tab, preferred_element_type=jnp.float32).reshape(
        2, num_rows, -1
    )
    real_part = cos_part[0] + sin_part[1]
    imag_part = cos_part[1] - sin_part[0]
    return jnp.stack([real_part, imag_part]).astype(jnp.bfloat16)


def cross_power(own_block, other_block):
    own_f = own_block.astype(jnp.float32)
    other_f = other_block.astype(jnp.float32)
    return jnp.sum(own_f[0] * other_f[0] + own_f[1] * other_f[1], axis=0)


def per_device(visibility, delay_kbin, block_bin, bin_slot, pair_flags):
    num_times = visibility.shape[1]
    num_rows = visibility.shape[2]
    num_chans = visibility.shape[3]
    num_kbins = num_chans // 2
    num_bins = bin_slot.shape[0]
    cycle_len = pair_flags.shape[0]
    cos_tab, sin_tab = delay_tables(num_chans)
    spectra = delay_transform(
        visibility.reshape(2, num_times * num_rows, num_chans), cos_tab, sin_tab
    )
    my_block = lax.axis_index("bl")
    num_blocks = lax.axis_size("bl")
    group = cycle_len
    position = my_block % group
    below_group = shifted(spectra, "bl", group)
    ahead = [spectra]
    behind = [spectra]
    for _ in range(group // 2):
        ahead.append(group_shifted(ahead[-1], "bl", group, -1))
    for _ in range(group - 1 - group // 2):
        behind.append(group_shifted(behind[-1], "bl", group, 1))
    offsets = jnp.arange(1, cycle_len + 1, dtype=jnp.int32)
    partner_pos = (position + offsets) % group
    owners = my_block - position + partner_pos
    flags = pair_flags[offsets - 1, owners]
    power_rows = []
    for offset in range(1, cycle_len + 1):
        if offset == group:
            held = spectra
        elif offset <= group // 2:
            held = ahead[offset]
        else:
            held = behind[group - offset]
        pair_power = cross_power(held, below_group)
        if offset < group:
            pair_power = jnp.where(
                position + offset < group, cross_power(held, spectra), pair_power
            )
        power_rows.append(flags[offset - 1].astype(jnp.float32) * pair_power)
    power_table = jnp.stack(power_rows)
    k_onehot = (delay_kbin[:, None] == jnp.arange(num_kbins, dtype=jnp.int32)[None, :]).astype(
        jnp.float32
    )
    scale_value = 1.0 / math.sqrt(num_rows * num_times * lax.axis_size("ta"))
    binned = jnp.dot(power_table, k_onehot, precision=lax.Precision.HIGHEST) * scale_value
    target_rows = bin_slot[block_bin[owners]]
    slot_onehot = (
        jnp.arange(num_bins, dtype=jnp.int32)[:, None] == target_rows[None, :]
    ).astype(jnp.float32)
    partial_table = jnp.sum(slot_onehot[:, :, None] * binned[None, :, :], axis=1)
    received = lax.all_to_all(partial_table, "bl", 0, 0, tiled=True)
    return lax.psum(jnp.sum(received, axis=0, keepdims=True), "ta")


def solution(mesh):
    placed = (P(None, "ta", "bl", None), P(), P(), P(), P())
    return jax.shard_map(
        per_device, mesh=mesh, in_specs=placed, out_specs=P("bl", None), check_vma=False
    )
```

```python
import math

import ml_dtypes
import numpy as np

import jax
import jax.numpy as jnp
from jax import lax
from jax.sharding import PartitionSpec as P


def shifted(block, axis, distance):
    devices = range(lax.axis_size(axis))
    route = [((i - distance) % len(devices), i) for i in devices]
    return lax.ppermute(block, axis, route)


def group_shifted(block, axis, group, distance):
    devices = range(lax.axis_size(axis))
    route = [(i, i - i % group + (i + distance) % group) for i in devices]
    return lax.ppermute(block, axis, route)


def delay_tables(num_chans):
    chan_idx = np.arange(num_chans, dtype=np.int32)
    phase_idx = chan_idx[:, None] * chan_idx[None, :] % num_chans
    step_angle = np.float32(2.0 * math.pi / num_chans)
    phase_angle = step_angle * phase_idx.astype(np.float32)
    base_angle = step_angle * chan_idx.astype(np.float32)

    def cos32(angle):
        return np.cos(angle.astype(np.float64)).astype(np.float32)

    taper_win = (
        np.float32(0.35875)
        - np.float32(0.48829) * cos32(base_angle)
        + np.float32(0.14128) * cos32(np.float32(2.0) * base_angle)
        - np.float32(0.01168) * cos32(np.float32(3.0) * base_angle)
    )
    scale_norm = np.float32(1.0) / np.sqrt(np.sum(taper_win * taper_win, dtype=np.float32))
    weight_col = (taper_win * scale_norm)[:, None]
    cos_tab = (weight_col * cos32(phase_angle)).astype(ml_dtypes.bfloat16)
    sin_tab = (weight_col * np.sin(phase_angle.astype(np.float64)).astype(np.float32)).astype(
        ml_dtypes.bfloat16
    )
    return (jnp.asarray(cos_tab), jnp.asarray(sin_tab))


def delay_transform(block_data, cos_tab, sin_tab):
    num_rows = block_data.shape[1]
    flat_rows = block_data.reshape(2 * num_rows, block_data.shape[2])
    cos_part = jnp.dot(flat_rows, cos_tab, preferred_element_type=jnp.float32).reshape(
        2, num_rows, -1
    )
    sin_part = jnp.dot(flat_rows, sin_tab, preferred_element_type=jnp.float32).reshape(
        2, num_rows, -1
    )
    real_part = cos_part[0] + sin_part[1]
    imag_part = cos_part[1] - sin_part[0]
    return jnp.stack([real_part, imag_part]).astype(jnp.bfloat16)


def cross_power(own_block, other_block):
    own_f = own_block.astype(jnp.float32)
    other_f = other_block.astype(jnp.float32)
    return jnp.sum(own_f[0] * other_f[0] + own_f[1] * other_f[1], axis=0)


def per_device(visibility, delay_kbin, block_bin, bin_slot, pair_flags):
    num_times = visibility.shape[1]
    num_rows = visibility.shape[2]
    num_chans = visibility.shape[3]
    num_kbins = num_chans // 2
    num_bins = bin_slot.shape[0]
    cycle_len = pair_flags.shape[0]
    cos_tab, sin_tab = delay_tables(num_chans)
    spectra = delay_transform(
        visibility.reshape(2, num_times * num_rows, num_chans), cos_tab, sin_tab
    )
    my_block = lax.axis_index("bl")
    num_blocks = lax.axis_size("bl")
    group = cycle_len
    position = my_block % group
    split = num_chans // 2
    below_low = shifted(spectra[:, :, :split], "bl", group)
    above_high = shifted(spectra[:, :, split:], "bl", -group)
    ahead = [spectra]
    behind = [spectra]
    for _ in range(group // 2):
        ahead.append(group_shifted(ahead[-1], "bl", group, -1))
    for _ in range(group - 1 - group // 2):
        behind.append(group_shifted(behind[-1], "bl", group, 1))
    offsets = jnp.arange(1, cycle_len + 1, dtype=jnp.int32)
    partner_pos = (position + offsets) % group
    owners = my_block - position + partner_pos
    flags = pair_flags[offsets - 1, owners].astype(jnp.float32)
    up_owner = (my_block + group) % num_blocks
    up_flags = pair_flags[:, up_owner].astype(jnp.float32)
    upper_half = jnp.zeros((split,), jnp.float32)
    power_rows = []
    for offset in range(1, cycle_len + 1):
        if offset == group:
            held = spectra
        elif offset <= group // 2:
            held = ahead[offset]
        else:
            held = behind[group - offset]
        low_half = cross_power(held[:, :, :split], below_low)
        pair_power = jnp.concatenate([low_half, jnp.zeros((num_chans - split,), jnp.float32)])
        if offset < group:
            pair_power = jnp.where(
                position + offset < group, cross_power(held, spectra), pair_power
            )
        power_rows.append(flags[offset - 1] * pair_power)
        reach = offset % group
        upper_half = upper_half + jnp.where(
            position + reach < group,
            up_flags[group - reach - 1] * cross_power(above_high, held[:, :, split:]),
            0.0,
        )
    power_rows.append(jnp.concatenate([jnp.zeros((split,), jnp.float32), upper_half]))
    owners = jnp.concatenate([owners, up_owner[None]])
    power_table = jnp.stack(power_rows)
    k_onehot = (delay_kbin[:, None] == jnp.arange(num_kbins, dtype=jnp.int32)[None, :]).astype(
        jnp.float32
    )
    scale_value = 1.0 / math.sqrt(num_rows * num_times * lax.axis_size("ta"))
    binned = jnp.dot(power_table, k_onehot, precision=lax.Precision.HIGHEST) * scale_value
    target_rows = bin_slot[block_bin[owners]]
    slot_onehot = (
        jnp.arange(num_bins, dtype=jnp.int32)[:, None] == target_rows[None, :]
    ).astype(jnp.float32)
    partial_table = jnp.sum(slot_onehot[:, :, None] * binned[None, :, :], axis=1)
    received = lax.all_to_all(partial_table, "bl", 0, 0, tiled=True)
    return lax.psum(jnp.sum(received, axis=0, keepdims=True), "ta")


def solution(mesh):
    placed = (P(None, "ta", "bl", None), P(), P(), P(), P())
    return jax.shard_map(
        per_device, mesh=mesh, in_specs=placed, out_specs=P("bl", None), check_vma=False
    )
```

```python
import math

import ml_dtypes
import numpy as np

import jax
import jax.numpy as jnp
from jax import lax
from jax.sharding import PartitionSpec as P


def shifted(block, axis, distance):
    devices = range(lax.axis_size(axis))
    route = [((i - distance) % len(devices), i) for i in devices]
    return lax.ppermute(block, axis, route)


def group_shifted(block, axis, group, distance):
    devices = range(lax.axis_size(axis))
    route = [(i, i - i % group + (i + distance) % group) for i in devices]
    return lax.ppermute(block, axis, route)


def delay_tables(num_chans):
    chan_idx = np.arange(num_chans, dtype=np.int32)
    phase_idx = chan_idx[:, None] * chan_idx[None, :] % num_chans
    step_angle = np.float32(2.0 * math.pi / num_chans)
    phase_angle = step_angle * phase_idx.astype(np.float32)
    base_angle = step_angle * chan_idx.astype(np.float32)

    def cos32(angle):
        return np.cos(angle.astype(np.float64)).astype(np.float32)

    taper_win = (
        np.float32(0.35875)
        - np.float32(0.48829) * cos32(base_angle)
        + np.float32(0.14128) * cos32(np.float32(2.0) * base_angle)
        - np.float32(0.01168) * cos32(np.float32(3.0) * base_angle)
    )
    scale_norm = np.float32(1.0) / np.sqrt(np.sum(taper_win * taper_win, dtype=np.float32))
    weight_col = (taper_win * scale_norm)[:, None]
    cos_tab = (weight_col * cos32(phase_angle)).astype(ml_dtypes.bfloat16)
    sin_tab = (weight_col * np.sin(phase_angle.astype(np.float64)).astype(np.float32)).astype(
        ml_dtypes.bfloat16
    )
    return (jnp.asarray(cos_tab), jnp.asarray(sin_tab))


def delay_transform(block_data, cos_tab, sin_tab):
    num_rows = block_data.shape[1]
    flat_rows = block_data.reshape(2 * num_rows, block_data.shape[2])
    cos_part = jnp.dot(flat_rows, cos_tab, preferred_element_type=jnp.float32).reshape(
        2, num_rows, -1
    )
    sin_part = jnp.dot(flat_rows, sin_tab, preferred_element_type=jnp.float32).reshape(
        2, num_rows, -1
    )
    real_part = cos_part[0] + sin_part[1]
    imag_part = cos_part[1] - sin_part[0]
    return jnp.stack([real_part, imag_part]).astype(jnp.bfloat16)


def cross_power(own_block, other_block):
    own_f = own_block.astype(jnp.float32)
    other_f = other_block.astype(jnp.float32)
    return jnp.sum(own_f[0] * other_f[0] + own_f[1] * other_f[1], axis=0)


def per_device(visibility, delay_kbin, block_bin, bin_slot, pair_flags):
    num_times = visibility.shape[1]
    num_rows = visibility.shape[2]
    num_chans = visibility.shape[3]
    num_kbins = num_chans // 2
    num_bins = bin_slot.shape[0]
    cycle_len = pair_flags.shape[0]
    cos_tab, sin_tab = delay_tables(num_chans)
    spectra = delay_transform(
        visibility.reshape(2, num_times * num_rows, num_chans), cos_tab, sin_tab
    )
    my_block = lax.axis_index("bl")
    num_blocks = lax.axis_size("bl")
    group = cycle_len
    position = my_block % group
    below_group = shifted(spectra, "bl", group)
    ahead = [spectra]
    behind = [spectra]
    for _ in range(group // 2):
        ahead.append(group_shifted(ahead[-1], "bl", group, -1))
    for _ in range(group - 1 - group // 2):
        behind.append(group_shifted(behind[-1], "bl", group, 1))
    offsets = jnp.arange(1, cycle_len + 1, dtype=jnp.int32)
    partner_pos = (position + offsets) % group
    owners = my_block - position + partner_pos
    flags = pair_flags[offsets - 1, owners]
    held_blocks = []
    for offset in range(1, cycle_len + 1):
        if offset == group:
            held_blocks.append(spectra)
        elif offset <= group // 2:
            held_blocks.append(ahead[offset])
        else:
            held_blocks.append(behind[group - offset])
    inner_power = lax.optimization_barrier(
        [cross_power(held, spectra) for held in held_blocks[:-1]]
    )
    below_group, held_blocks = lax.optimization_barrier((below_group, held_blocks))
    power_rows = []
    for offset in range(1, cycle_len + 1):
        pair_power = cross_power(held_blocks[offset - 1], below_group)
        if offset < group:
            pair_power = jnp.where(position + offset < group, inner_power[offset - 1], pair_power)
        power_rows.append(flags[offset - 1].astype(jnp.float32) * pair_power)
    power_table = jnp.stack(power_rows)
    k_onehot = (delay_kbin[:, None] == jnp.arange(num_kbins, dtype=jnp.int32)[None, :]).astype(
        jnp.float32
    )
    scale_value = 1.0 / math.sqrt(num_rows * num_times * lax.axis_size("ta"))
    binned = jnp.dot(power_table, k_onehot, precision=lax.Precision.HIGHEST) * scale_value
    target_rows = bin_slot[block_bin[owners]]
    slot_onehot = (
        jnp.arange(num_bins, dtype=jnp.int32)[:, None] == target_rows[None, :]
    ).astype(jnp.float32)
    partial_table = jnp.sum(slot_onehot[:, :, None] * binned[None, :, :], axis=1)
    received = lax.all_to_all(partial_table, "bl", 0, 0, tiled=True)
    return lax.psum(jnp.sum(received, axis=0, keepdims=True), "ta")


def solution(mesh):
    placed = (P(None, "ta", "bl", None), P(), P(), P(), P())
    return jax.shard_map(
        per_device, mesh=mesh, in_specs=placed, out_specs=P("bl", None), check_vma=False
    )
```

```python
import math

import ml_dtypes
import numpy as np

import jax
import jax.numpy as jnp
from jax import lax
from jax.sharding import PartitionSpec as P


def shifted(block, axis, distance):
    devices = range(lax.axis_size(axis))
    route = [((i - distance) % len(devices), i) for i in devices]
    return lax.ppermute(block, axis, route)


def group_shifted(block, axis, group, distance):
    devices = range(lax.axis_size(axis))
    route = [(i, i - i % group + (i + distance) % group) for i in devices]
    return lax.ppermute(block, axis, route)


def delay_tables(num_chans):
    chan_idx = np.arange(num_chans, dtype=np.int32)
    phase_idx = chan_idx[:, None] * chan_idx[None, :] % num_chans
    step_angle = np.float32(2.0 * math.pi / num_chans)
    phase_angle = step_angle * phase_idx.astype(np.float32)
    base_angle = step_angle * chan_idx.astype(np.float32)

    def cos32(angle):
        return np.cos(angle.astype(np.float64)).astype(np.float32)

    taper_win = (
        np.float32(0.35875)
        - np.float32(0.48829) * cos32(base_angle)
        + np.float32(0.14128) * cos32(np.float32(2.0) * base_angle)
        - np.float32(0.01168) * cos32(np.float32(3.0) * base_angle)
    )
    scale_norm = np.float32(1.0) / np.sqrt(np.sum(taper_win * taper_win, dtype=np.float32))
    weight_col = (taper_win * scale_norm)[:, None]
    cos_tab = (weight_col * cos32(phase_angle)).astype(ml_dtypes.bfloat16)
    sin_tab = (weight_col * np.sin(phase_angle.astype(np.float64)).astype(np.float32)).astype(
        ml_dtypes.bfloat16
    )
    return (jnp.asarray(cos_tab), jnp.asarray(sin_tab))


def delay_transform(block_data, cos_tab, sin_tab):
    num_rows = block_data.shape[1]
    flat_rows = block_data.reshape(2 * num_rows, block_data.shape[2])
    cos_part = jnp.dot(flat_rows, cos_tab, preferred_element_type=jnp.float32).reshape(
        2, num_rows, -1
    )
    sin_part = jnp.dot(flat_rows, sin_tab, preferred_element_type=jnp.float32).reshape(
        2, num_rows, -1
    )
    real_part = cos_part[0] + sin_part[1]
    imag_part = cos_part[1] - sin_part[0]
    return jnp.stack([real_part, imag_part]).astype(jnp.bfloat16)


def cross_power(own_block, other_block):
    own_f = own_block.astype(jnp.float32)
    other_f = other_block.astype(jnp.float32)
    return jnp.sum(own_f[0] * other_f[0] + own_f[1] * other_f[1], axis=0)


def per_device(visibility, delay_kbin, block_bin, bin_slot, pair_flags):
    num_times = visibility.shape[1]
    num_rows = visibility.shape[2]
    num_chans = visibility.shape[3]
    num_kbins = num_chans // 2
    num_bins = bin_slot.shape[0]
    cycle_len = pair_flags.shape[0]
    cos_tab, sin_tab = delay_tables(num_chans)
    spectra = delay_transform(
        visibility.reshape(2, num_times * num_rows, num_chans), cos_tab, sin_tab
    )
    my_block = lax.axis_index("bl")
    num_blocks = lax.axis_size("bl")
    group = cycle_len
    position = my_block % group
    below_group = shifted(spectra, "bl", group)
    ahead = [spectra]
    behind = [spectra]
    for _ in range(group // 2):
        ahead.append(group_shifted(ahead[-1], "bl", group, -1))
    for _ in range(group - 1 - group // 2):
        behind.append(group_shifted(behind[-1], "bl", group, 1))
    offsets = jnp.arange(1, cycle_len + 1, dtype=jnp.int32)
    partner_pos = (position + offsets) % group
    owners = my_block - position + partner_pos
    flags = pair_flags[offsets - 1, owners]
    held_blocks = []
    for offset in range(1, cycle_len + 1):
        if offset == group:
            held_blocks.append(spectra)
        elif offset <= group // 2:
            held_blocks.append(ahead[offset])
        else:
            held_blocks.append(behind[group - offset])
    inner_power = lax.optimization_barrier(
        [cross_power(held, spectra) for held in held_blocks[:-1]]
    )
    below_group, ahead[3], behind[3] = lax.optimization_barrier((below_group, ahead[3], behind[3]))
    power_rows = []
    for offset in range(1, cycle_len + 1):
        pair_power = cross_power(held_blocks[offset - 1], below_group)
        if offset < group:
            pair_power = jnp.where(position + offset < group, inner_power[offset - 1], pair_power)
        power_rows.append(flags[offset - 1].astype(jnp.float32) * pair_power)
    power_table = jnp.stack(power_rows)
    k_onehot = (delay_kbin[:, None] == jnp.arange(num_kbins, dtype=jnp.int32)[None, :]).astype(
        jnp.float32
    )
    scale_value = 1.0 / math.sqrt(num_rows * num_times * lax.axis_size("ta"))
    binned = jnp.dot(power_table, k_onehot, precision=lax.Precision.HIGHEST) * scale_value
    target_rows = bin_slot[block_bin[owners]]
    slot_onehot = (
        jnp.arange(num_bins, dtype=jnp.int32)[:, None] == target_rows[None, :]
    ).astype(jnp.float32)
    partial_table = jnp.sum(slot_onehot[:, :, None] * binned[None, :, :], axis=1)
    received = lax.all_to_all(partial_table, "bl", 0, 0, tiled=True)
    return lax.psum(jnp.sum(received, axis=0, keepdims=True), "ta")


def solution(mesh):
    placed = (P(None, "ta", "bl", None), P(), P(), P(), P())
    return jax.shard_map(
        per_device, mesh=mesh, in_specs=placed, out_specs=P("bl", None), check_vma=False
    )
```

```python
import math

import ml_dtypes
import numpy as np

import jax
import jax.numpy as jnp
from jax import lax
from jax.sharding import PartitionSpec as P


def shifted(block, axis, distance):
    devices = range(lax.axis_size(axis))
    route = [((i - distance) % len(devices), i) for i in devices]
    return lax.ppermute(block, axis, route)


def group_shifted(block, axis, group, distance):
    devices = range(lax.axis_size(axis))
    route = [(i, i - i % group + (i + distance) % group) for i in devices]
    return lax.ppermute(block, axis, route)


def vertical_import(block, group):
    num_blocks = lax.axis_size("bl")
    num_ta = lax.axis_size("ta")
    z_ring = 2 * num_ta

    def flat(bl, ta):
        return bl * num_ta + ta

    def down_z(bl, ta):
        z_hi = (bl // group) % 2
        z = (z_hi * num_ta + ta - 1) % z_ring
        new_bl = bl + ((z // num_ta) - z_hi) * group
        return new_bl, z % num_ta

    pairs = [(b, t) for b in range(num_blocks) for t in range(num_ta)]
    target = {(b, t): ((b + group) % num_blocks, t) for b, t in pairs}
    direct = [(flat(*p), flat(*target[p])) for p in pairs]
    to_relay = [(flat(*p), flat(*down_z(*p))) for p in pairs]
    from_relay = [(flat(*down_z(*p)), flat(*target[p])) for p in pairs]
    split = block.shape[-1] // 2
    axes = ("bl", "ta")
    low = lax.ppermute(block[..., :split], axes, direct)
    high = lax.ppermute(lax.ppermute(block[..., split:], axes, to_relay), axes, from_relay)
    return jnp.concatenate([low, high], axis=-1)


def delay_tables(num_chans):
    chan_idx = np.arange(num_chans, dtype=np.int32)
    phase_idx = chan_idx[:, None] * chan_idx[None, :] % num_chans
    step_angle = np.float32(2.0 * math.pi / num_chans)
    phase_angle = step_angle * phase_idx.astype(np.float32)
    base_angle = step_angle * chan_idx.astype(np.float32)

    def cos32(angle):
        return np.cos(angle.astype(np.float64)).astype(np.float32)

    taper_win = (
        np.float32(0.35875)
        - np.float32(0.48829) * cos32(base_angle)
        + np.float32(0.14128) * cos32(np.float32(2.0) * base_angle)
        - np.float32(0.01168) * cos32(np.float32(3.0) * base_angle)
    )
    scale_norm = np.float32(1.0) / np.sqrt(np.sum(taper_win * taper_win, dtype=np.float32))
    weight_col = (taper_win * scale_norm)[:, None]
    cos_tab = (weight_col * cos32(phase_angle)).astype(ml_dtypes.bfloat16)
    sin_tab = (weight_col * np.sin(phase_angle.astype(np.float64)).astype(np.float32)).astype(
        ml_dtypes.bfloat16
    )
    return (jnp.asarray(cos_tab), jnp.asarray(sin_tab))


def delay_transform(block_data, cos_tab, sin_tab):
    num_rows = block_data.shape[1]
    flat_rows = block_data.reshape(2 * num_rows, block_data.shape[2])
    cos_part = jnp.dot(flat_rows, cos_tab, preferred_element_type=jnp.float32).reshape(
        2, num_rows, -1
    )
    sin_part = jnp.dot(flat_rows, sin_tab, preferred_element_type=jnp.float32).reshape(
        2, num_rows, -1
    )
    real_part = cos_part[0] + sin_part[1]
    imag_part = cos_part[1] - sin_part[0]
    return jnp.stack([real_part, imag_part]).astype(jnp.bfloat16)


def cross_power(own_block, other_block):
    own_f = own_block.astype(jnp.float32)
    other_f = other_block.astype(jnp.float32)
    return jnp.sum(own_f[0] * other_f[0] + own_f[1] * other_f[1], axis=0)


def per_device(visibility, delay_kbin, block_bin, bin_slot, pair_flags):
    num_times = visibility.shape[1]
    num_rows = visibility.shape[2]
    num_chans = visibility.shape[3]
    num_kbins = num_chans // 2
    num_bins = bin_slot.shape[0]
    cycle_len = pair_flags.shape[0]
    cos_tab, sin_tab = delay_tables(num_chans)
    spectra = delay_transform(
        visibility.reshape(2, num_times * num_rows, num_chans), cos_tab, sin_tab
    )
    my_block = lax.axis_index("bl")
    num_blocks = lax.axis_size("bl")
    group = cycle_len
    position = my_block % group
    below_group = vertical_import(spectra, group)
    ahead = [spectra]
    behind = [spectra]
    for _ in range(group // 2):
        ahead.append(group_shifted(ahead[-1], "bl", group, -1))
    for _ in range(group - 1 - group // 2):
        behind.append(group_shifted(behind[-1], "bl", group, 1))
    offsets = jnp.arange(1, cycle_len + 1, dtype=jnp.int32)
    partner_pos = (position + offsets) % group
    owners = my_block - position + partner_pos
    flags = pair_flags[offsets - 1, owners]
    power_rows = []
    for offset in range(1, cycle_len + 1):
        if offset == group:
            held = spectra
        elif offset <= group // 2:
            held = ahead[offset]
        else:
            held = behind[group - offset]
        pair_power = cross_power(held, below_group)
        if offset < group:
            pair_power = jnp.where(
                position + offset < group, cross_power(held, spectra), pair_power
            )
        power_rows.append(flags[offset - 1].astype(jnp.float32) * pair_power)
    power_table = jnp.stack(power_rows)
    k_onehot = (delay_kbin[:, None] == jnp.arange(num_kbins, dtype=jnp.int32)[None, :]).astype(
        jnp.float32
    )
    scale_value = 1.0 / math.sqrt(num_rows * num_times * lax.axis_size("ta"))
    binned = jnp.dot(power_table, k_onehot, precision=lax.Precision.HIGHEST) * scale_value
    target_rows = bin_slot[block_bin[owners]]
    slot_onehot = (
        jnp.arange(num_bins, dtype=jnp.int32)[:, None] == target_rows[None, :]
    ).astype(jnp.float32)
    partial_table = jnp.sum(slot_onehot[:, :, None] * binned[None, :, :], axis=1)
    received = lax.all_to_all(partial_table, "bl", 0, 0, tiled=True)
    return lax.psum(jnp.sum(received, axis=0, keepdims=True), "ta")


def solution(mesh):
    placed = (P(None, "ta", "bl", None), P(), P(), P(), P())
    return jax.shard_map(
        per_device, mesh=mesh, in_specs=placed, out_specs=P("bl", None), check_vma=False
    )
```

```python
import math

import ml_dtypes
import numpy as np

import jax
import jax.numpy as jnp
from jax import lax
from jax.sharding import PartitionSpec as P


def shifted(block, axis, distance):
    devices = range(lax.axis_size(axis))
    route = [((i - distance) % len(devices), i) for i in devices]
    return lax.ppermute(block, axis, route)


def group_shifted(block, axis, group, distance):
    devices = range(lax.axis_size(axis))
    route = [(i, i - i % group + (i + distance) % group) for i in devices]
    return lax.ppermute(block, axis, route)


def delay_tables(num_chans):
    chan_idx = np.arange(num_chans, dtype=np.int32)
    phase_idx = chan_idx[:, None] * chan_idx[None, :] % num_chans
    step_angle = np.float32(2.0 * math.pi / num_chans)
    phase_angle = step_angle * phase_idx.astype(np.float32)
    base_angle = step_angle * chan_idx.astype(np.float32)

    def cos32(angle):
        return np.cos(angle.astype(np.float64)).astype(np.float32)

    taper_win = (
        np.float32(0.35875)
        - np.float32(0.48829) * cos32(base_angle)
        + np.float32(0.14128) * cos32(np.float32(2.0) * base_angle)
        - np.float32(0.01168) * cos32(np.float32(3.0) * base_angle)
    )
    scale_norm = np.float32(1.0) / np.sqrt(np.sum(taper_win * taper_win, dtype=np.float32))
    weight_col = (taper_win * scale_norm)[:, None]
    cos_tab = (weight_col * cos32(phase_angle)).astype(ml_dtypes.bfloat16)
    sin_tab = (weight_col * np.sin(phase_angle.astype(np.float64)).astype(np.float32)).astype(
        ml_dtypes.bfloat16
    )
    return (jnp.asarray(cos_tab), jnp.asarray(sin_tab))


def delay_transform(block_data, cos_tab, sin_tab):
    num_rows = block_data.shape[1]
    flat_rows = block_data.reshape(2 * num_rows, block_data.shape[2])
    cos_part = jnp.dot(flat_rows, cos_tab, preferred_element_type=jnp.float32).reshape(
        2, num_rows, -1
    )
    sin_part = jnp.dot(flat_rows, sin_tab, preferred_element_type=jnp.float32).reshape(
        2, num_rows, -1
    )
    real_part = cos_part[0] + sin_part[1]
    imag_part = cos_part[1] - sin_part[0]
    return jnp.stack([real_part, imag_part]).astype(jnp.bfloat16)


def cross_power(own_block, other_block):
    own_f = own_block.astype(jnp.float32)
    other_f = other_block.astype(jnp.float32)
    return jnp.sum(own_f[0] * other_f[0] + own_f[1] * other_f[1], axis=0)


def per_device(visibility, delay_kbin, block_bin, bin_slot, pair_flags):
    num_times = visibility.shape[1]
    num_rows = visibility.shape[2]
    num_chans = visibility.shape[3]
    num_kbins = num_chans // 2
    num_bins = bin_slot.shape[0]
    cycle_len = pair_flags.shape[0]
    cos_tab, sin_tab = delay_tables(num_chans)
    spectra = delay_transform(
        visibility.reshape(2, num_times * num_rows, num_chans), cos_tab, sin_tab
    )
    my_block = lax.axis_index("bl")
    num_blocks = lax.axis_size("bl")
    group = cycle_len
    position = my_block % group
    split = num_chans // 2
    below_low = shifted(spectra[:, :, :split], "bl", group)
    below_high = shifted(spectra[:, :, split:], "bl", group)
    ahead = [spectra]
    behind = [spectra]
    for _ in range(group // 2):
        ahead.append(group_shifted(ahead[-1], "bl", group, -1))
    for _ in range(group - 1 - group // 2):
        behind.append(group_shifted(behind[-1], "bl", group, 1))
    offsets = jnp.arange(1, cycle_len + 1, dtype=jnp.int32)
    partner_pos = (position + offsets) % group
    owners = my_block - position + partner_pos
    flags = pair_flags[offsets - 1, owners]
    held_blocks = []
    for offset in range(1, cycle_len + 1):
        if offset == group:
            held_blocks.append(spectra)
        elif offset <= group // 2:
            held_blocks.append(ahead[offset])
        else:
            held_blocks.append(behind[group - offset])
    below_low, ahead[2] = lax.optimization_barrier((below_low, ahead[2]))
    low_power = [cross_power(held[:, :, :split], below_low) for held in held_blocks]
    below_high, ahead[4] = lax.optimization_barrier((below_high, ahead[4]))
    power_rows = []
    for offset in range(1, cycle_len + 1):
        held = held_blocks[offset - 1]
        high = cross_power(held[:, :, split:], below_high)
        pair_power = jnp.concatenate([low_power[offset - 1], high])
        if offset < group:
            pair_power = jnp.where(
                position + offset < group, cross_power(held, spectra), pair_power
            )
        power_rows.append(flags[offset - 1].astype(jnp.float32) * pair_power)
    power_table = jnp.stack(power_rows)
    k_onehot = (delay_kbin[:, None] == jnp.arange(num_kbins, dtype=jnp.int32)[None, :]).astype(
        jnp.float32
    )
    scale_value = 1.0 / math.sqrt(num_rows * num_times * lax.axis_size("ta"))
    binned = jnp.dot(power_table, k_onehot, precision=lax.Precision.HIGHEST) * scale_value
    target_rows = bin_slot[block_bin[owners]]
    slot_onehot = (
        jnp.arange(num_bins, dtype=jnp.int32)[:, None] == target_rows[None, :]
    ).astype(jnp.float32)
    partial_table = jnp.sum(slot_onehot[:, :, None] * binned[None, :, :], axis=1)
    received = lax.all_to_all(partial_table, "bl", 0, 0, tiled=True)
    return lax.psum(jnp.sum(received, axis=0, keepdims=True), "ta")


def solution(mesh):
    placed = (P(None, "ta", "bl", None), P(), P(), P(), P())
    return jax.shard_map(
        per_device, mesh=mesh, in_specs=placed, out_specs=P("bl", None), check_vma=False
    )
```

```python
import math

import ml_dtypes
import numpy as np

import jax
import jax.numpy as jnp
from jax import lax
from jax.sharding import PartitionSpec as P


def shifted(block, axis, distance):
    devices = range(lax.axis_size(axis))
    route = [((i - distance) % len(devices), i) for i in devices]
    return lax.ppermute(block, axis, route)


def group_shifted(block, axis, group, distance):
    devices = range(lax.axis_size(axis))
    route = [(i, i - i % group + (i + distance) % group) for i in devices]
    return lax.ppermute(block, axis, route)


def delay_tables(num_chans):
    chan_idx = np.arange(num_chans, dtype=np.int32)
    phase_idx = chan_idx[:, None] * chan_idx[None, :] % num_chans
    step_angle = np.float32(2.0 * math.pi / num_chans)
    phase_angle = step_angle * phase_idx.astype(np.float32)
    base_angle = step_angle * chan_idx.astype(np.float32)

    def cos32(angle):
        return np.cos(angle.astype(np.float64)).astype(np.float32)

    taper_win = (
        np.float32(0.35875)
        - np.float32(0.48829) * cos32(base_angle)
        + np.float32(0.14128) * cos32(np.float32(2.0) * base_angle)
        - np.float32(0.01168) * cos32(np.float32(3.0) * base_angle)
    )
    scale_norm = np.float32(1.0) / np.sqrt(np.sum(taper_win * taper_win, dtype=np.float32))
    weight_col = (taper_win * scale_norm)[:, None]
    cos_tab = (weight_col * cos32(phase_angle)).astype(ml_dtypes.bfloat16)
    sin_tab = (weight_col * np.sin(phase_angle.astype(np.float64)).astype(np.float32)).astype(
        ml_dtypes.bfloat16
    )
    return (jnp.asarray(cos_tab), jnp.asarray(sin_tab))


def delay_transform(block_data, cos_tab, sin_tab):
    num_rows = block_data.shape[1]
    flat_rows = block_data.reshape(2 * num_rows, block_data.shape[2])
    cos_part = jnp.dot(flat_rows, cos_tab, preferred_element_type=jnp.float32).reshape(
        2, num_rows, -1
    )
    sin_part = jnp.dot(flat_rows, sin_tab, preferred_element_type=jnp.float32).reshape(
        2, num_rows, -1
    )
    real_part = cos_part[0] + sin_part[1]
    imag_part = cos_part[1] - sin_part[0]
    return jnp.stack([real_part, imag_part]).astype(jnp.bfloat16)


def cross_power(own_block, other_block):
    own_f = own_block.astype(jnp.float32)
    other_f = other_block.astype(jnp.float32)
    return jnp.sum(own_f[0] * other_f[0] + own_f[1] * other_f[1], axis=0)


def per_device(visibility, delay_kbin, block_bin, bin_slot, pair_flags):
    num_times = visibility.shape[1]
    num_rows = visibility.shape[2]
    num_chans = visibility.shape[3]
    num_kbins = num_chans // 2
    num_bins = bin_slot.shape[0]
    cycle_len = pair_flags.shape[0]
    cos_tab, sin_tab = delay_tables(num_chans)
    spectra = delay_transform(
        visibility.reshape(2, num_times * num_rows, num_chans), cos_tab, sin_tab
    )
    my_block = lax.axis_index("bl")
    num_blocks = lax.axis_size("bl")
    group = cycle_len
    position = my_block % group
    below_group = shifted(spectra, "bl", group)
    ahead = [spectra]
    behind = [spectra]
    for _ in range(group // 2):
        ahead.append(group_shifted(ahead[-1], "bl", group, -1))
    for step in range(group - 1 - group // 2):
        if step == 1:
            below_group, behind[-1] = lax.optimization_barrier((below_group, behind[-1]))
        behind.append(group_shifted(behind[-1], "bl", group, 1))
    offsets = jnp.arange(1, cycle_len + 1, dtype=jnp.int32)
    partner_pos = (position + offsets) % group
    owners = my_block - position + partner_pos
    flags = pair_flags[offsets - 1, owners]
    power_rows = []
    for offset in range(1, cycle_len + 1):
        if offset == group:
            held = spectra
        elif offset <= group // 2:
            held = ahead[offset]
        else:
            held = behind[group - offset]
        pair_power = cross_power(held, below_group)
        if offset < group:
            pair_power = jnp.where(
                position + offset < group, cross_power(held, spectra), pair_power
            )
        power_rows.append(flags[offset - 1].astype(jnp.float32) * pair_power)
    power_table = jnp.stack(power_rows)
    k_onehot = (delay_kbin[:, None] == jnp.arange(num_kbins, dtype=jnp.int32)[None, :]).astype(
        jnp.float32
    )
    scale_value = 1.0 / math.sqrt(num_rows * num_times * lax.axis_size("ta"))
    binned = jnp.dot(power_table, k_onehot, precision=lax.Precision.HIGHEST) * scale_value
    target_rows = bin_slot[block_bin[owners]]
    slot_onehot = (
        jnp.arange(num_bins, dtype=jnp.int32)[:, None] == target_rows[None, :]
    ).astype(jnp.float32)
    partial_table = jnp.sum(slot_onehot[:, :, None] * binned[None, :, :], axis=1)
    received = lax.all_to_all(partial_table, "bl", 0, 0, tiled=True)
    return lax.psum(jnp.sum(received, axis=0, keepdims=True), "ta")


def solution(mesh):
    placed = (P(None, "ta", "bl", None), P(), P(), P(), P())
    return jax.shard_map(
        per_device, mesh=mesh, in_specs=placed, out_specs=P("bl", None), check_vma=False
    )
```

```python
import math

import ml_dtypes
import numpy as np

import jax
import jax.numpy as jnp
from jax import lax
from jax.sharding import PartitionSpec as P


def shifted(block, axis, distance):
    devices = range(lax.axis_size(axis))
    route = [((i - distance) % len(devices), i) for i in devices]
    return lax.ppermute(block, axis, route)


def group_shifted(block, axis, group, distance):
    devices = range(lax.axis_size(axis))
    route = [(i, i - i % group + (i + distance) % group) for i in devices]
    return lax.ppermute(block, axis, route)


def delay_tables(num_chans):
    chan_idx = np.arange(num_chans, dtype=np.int32)
    phase_idx = chan_idx[:, None] * chan_idx[None, :] % num_chans
    step_angle = np.float32(2.0 * math.pi / num_chans)
    phase_angle = step_angle * phase_idx.astype(np.float32)
    base_angle = step_angle * chan_idx.astype(np.float32)

    def cos32(angle):
        return np.cos(angle.astype(np.float64)).astype(np.float32)

    taper_win = (
        np.float32(0.35875)
        - np.float32(0.48829) * cos32(base_angle)
        + np.float32(0.14128) * cos32(np.float32(2.0) * base_angle)
        - np.float32(0.01168) * cos32(np.float32(3.0) * base_angle)
    )
    scale_norm = np.float32(1.0) / np.sqrt(np.sum(taper_win * taper_win, dtype=np.float32))
    weight_col = (taper_win * scale_norm)[:, None]
    cos_tab = (weight_col * cos32(phase_angle)).astype(ml_dtypes.bfloat16)
    sin_tab = (weight_col * np.sin(phase_angle.astype(np.float64)).astype(np.float32)).astype(
        ml_dtypes.bfloat16
    )
    half = num_chans // 2
    cos_half, sin_half, cos_mid, sin_mid = lax.optimization_barrier(
        (
            jnp.asarray(cos_tab[:, :half]),
            jnp.asarray(sin_tab[:, :half]),
            jnp.asarray(cos_tab[:, half]),
            jnp.asarray(sin_tab[:, half]),
        )
    )
    cos_full = jnp.concatenate(
        [cos_half, cos_mid[:, None], cos_half[:, half - 1 : 0 : -1]], axis=1
    )
    sin_full = jnp.concatenate(
        [sin_half, sin_mid[:, None], -sin_half[:, half - 1 : 0 : -1]], axis=1
    )
    return (cos_full, sin_full)


def delay_transform(block_data, cos_tab, sin_tab):
    num_rows = block_data.shape[1]
    flat_rows = block_data.reshape(2 * num_rows, block_data.shape[2])
    cos_part = jnp.dot(flat_rows, cos_tab, preferred_element_type=jnp.float32).reshape(
        2, num_rows, -1
    )
    sin_part = jnp.dot(flat_rows, sin_tab, preferred_element_type=jnp.float32).reshape(
        2, num_rows, -1
    )
    real_part = cos_part[0] + sin_part[1]
    imag_part = cos_part[1] - sin_part[0]
    return jnp.stack([real_part, imag_part]).astype(jnp.bfloat16)


def cross_power(own_block, other_block):
    own_f = own_block.astype(jnp.float32)
    other_f = other_block.astype(jnp.float32)
    return jnp.sum(own_f[0] * other_f[0] + own_f[1] * other_f[1], axis=0)


def per_device(visibility, delay_kbin, block_bin, bin_slot, pair_flags):
    num_times = visibility.shape[1]
    num_rows = visibility.shape[2]
    num_chans = visibility.shape[3]
    num_kbins = num_chans // 2
    num_bins = bin_slot.shape[0]
    cycle_len = pair_flags.shape[0]
    cos_tab, sin_tab = delay_tables(num_chans)
    spectra = delay_transform(
        visibility.reshape(2, num_times * num_rows, num_chans), cos_tab, sin_tab
    )
    my_block = lax.axis_index("bl")
    num_blocks = lax.axis_size("bl")
    group = cycle_len
    position = my_block % group
    below_group = shifted(spectra, "bl", group)
    ahead = [spectra]
    behind = [spectra]
    for _ in range(group // 2):
        ahead.append(group_shifted(ahead[-1], "bl", group, -1))
    for step in range(group - 1 - group // 2):
        if step == 1:
            below_group, behind[-1] = lax.optimization_barrier((below_group, behind[-1]))
        behind.append(group_shifted(behind[-1], "bl", group, 1))
    offsets = jnp.arange(1, cycle_len + 1, dtype=jnp.int32)
    partner_pos = (position + offsets) % group
    owners = my_block - position + partner_pos
    flags = pair_flags[offsets - 1, owners]
    power_rows = []
    for offset in range(1, cycle_len + 1):
        if offset == group:
            held = spectra
        elif offset <= group // 2:
            held = ahead[offset]
        else:
            held = behind[group - offset]
        pair_power = cross_power(held, below_group)
        if offset < group:
            pair_power = jnp.where(
                position + offset < group, cross_power(held, spectra), pair_power
            )
        power_rows.append(flags[offset - 1].astype(jnp.float32) * pair_power)
    power_table = jnp.stack(power_rows)
    k_onehot = (delay_kbin[:, None] == jnp.arange(num_kbins, dtype=jnp.int32)[None, :]).astype(
        jnp.float32
    )
    scale_value = 1.0 / math.sqrt(num_rows * num_times * lax.axis_size("ta"))
    binned = jnp.dot(power_table, k_onehot, precision=lax.Precision.HIGHEST) * scale_value
    target_rows = bin_slot[block_bin[owners]]
    slot_onehot = (
        jnp.arange(num_bins, dtype=jnp.int32)[:, None] == target_rows[None, :]
    ).astype(jnp.float32)
    partial_table = jnp.sum(slot_onehot[:, :, None] * binned[None, :, :], axis=1)
    received = lax.all_to_all(partial_table, "bl", 0, 0, tiled=True)
    return lax.psum(jnp.sum(received, axis=0, keepdims=True), "ta")


def solution(mesh):
    placed = (P(None, "ta", "bl", None), P(), P(), P(), P())
    return jax.shard_map(
        per_device, mesh=mesh, in_specs=placed, out_specs=P("bl", None), check_vma=False
    )
```
